512 devices in a mesh: section: 8 (over z_hi, core), tp: 64 (over x, z_lo, y).
Axes of the slice: x: 4, y: 4, z: 16 (z_hi: 4, z_lo: 4; z = z_hi * 4 + z_lo), core: 2. Of those that a mesh axis runs over, the one named last changes fastest.
Arguments:
- incoming: bfloat16 [8, 320, 8192], P('section', None, 'tp'), may hold values from -6 to 6
- norm_gain: bfloat16 [8, 8192], P('section', 'tp'), may hold values from 0.5 to 1.5
- query_weight: bfloat16 [8, 8192, 8192], P('section', 'tp'), may hold values from -0.0625 to 0.0625
- query_scale: float32 [8, 64, 64], P('section', 'tp'), may hold values from 0.3 to 3
- query_keep: int32 [8, 64, 64], P('section', 'tp'), may hold values from 0 to 1, as said below
- kv_weight: bfloat16 [8, 8192, 2048], P('section', 'tp'), may hold values from -0.0625 to 0.0625
- kv_scale: float32 [8, 64, 16], P('section', 'tp'), may hold values from 0.3 to 3
- kv_keep: int32 [8, 64, 16], P('section', 'tp'), may hold values from 0 to 1, as said below
- out_weight: bfloat16 [8, 8192, 8192], P('section', 'tp'), may hold values from -0.0625 to 0.0625
- out_scale: float32 [8, 64, 64], P('section', 'tp'), may hold values from 0.3 to 3
- out_keep: int32 [8, 64, 64], P('section', 'tp'), may hold values from 0 to 1, as said below
- documents: int32 [320], replicated, may hold values from 0 to 3, never falling along the last dimension, each value on 1 to 160 neighbouring positions
Outputs:
- passed: bfloat16 [8, 320, 8192], P('section', None, 'tp')
The draws below stay inside these ranges and needn't reach their ends.
Inputs may be any that keep to these rules, and one draw needn't show every extreme that they name: `documents`: document numbers never fall along the tokens; every document has 1 to 160 tokens and one has exactly 160. `query_keep`: 1 keeps the block, 0 removes it. `kv_keep`: 1 keeps the block, 0 removes it. `out_keep`: 1 keeps the block, 0 removes it.
All inputs are finite; a program needn't handle non-finite values.
Results may differ from the reference program's by a relative error of at most 0.006.
Values may be sent and summed in bfloat16 or wider, within the bound.
No kernel may reach another device: no remote copies, remote signals or barrier semaphores. Data moves between devices by JAX's collectives and lax.ppermute only.
A program may use at most 64 MiB of HBM per device.

```python
import math
import jax
import jax.numpy as jnp
import numpy as np
from jax import lax

D = 8192
HEADS = 64
KV_HEADS = 8
HD = 128
BLK = 128
SPAN = 160
TOKENS = 320
LAYERS = 8


def keep_blocks(key, row_blocks, col_blocks):
    level_key = jax.random.fold_in(key, 11)
    entry_key = jax.random.fold_in(key, 12)
    levels = jax.random.randint(level_key, (LAYERS, row_blocks, 1), 1, 8)
    entries = jax.random.randint(entry_key, (LAYERS, row_blocks, col_blocks), 0, 8)
    return (entries < levels).astype(jnp.int32)


def draw_query_keep(key, part):
    return keep_blocks(jax.random.fold_in(key, 1), D // BLK, HEADS * HD // BLK)


def draw_kv_keep(key, part):
    return keep_blocks(jax.random.fold_in(key, 2), D // BLK, 2 * KV_HEADS * HD // BLK)


def draw_out_keep(key, part):
    return keep_blocks(jax.random.fold_in(key, 3), HEADS * HD // BLK, D // BLK)


def shard_levels(key, shape, pieces, least, largest):
    loudness = 1.0
    for axis_at, shards_of in pieces:
        draws = jax.random.uniform(jax.random.fold_in(jax.random.fold_in(key, 6), axis_at), (shards_of,), jnp.float32, least / len(pieces), largest / len(pieces))
        loudness = loudness * jnp.repeat(jnp.exp(draws), shape[axis_at] // shards_of).reshape((-1,) + (1,) * (len(shape) - 1 - axis_at))
    return loudness


def profile(number_of, total, bound, lean):
    loads = [(1 << 20) // math.isqrt(rank ** lean) + 1 for rank in range(2, number_of + 1)]
    rest, holding = total - bound - (number_of - 1), [1] * (number_of - 1)
    while rest > 0:
        movable = [i for i in range(number_of - 1) if holding[i] < bound]
        whole, left = sum([loads[i] for i in movable]), rest
        for i in movable:
            addition = min(bound - holding[i], max(1, left * loads[i] // whole), rest)
            holding[i] = holding[i] + addition
            rest = rest - addition
    return np.array([bound] + holding)


def uneven(key, count, total, bound, slope):
    if count == 2:
        one = jax.random.randint(key, (), max(1, total - bound), min(bound, total - 1) + 1)
        return jnp.stack([one, total - one])
    sizes = jnp.asarray(profile(count, total, bound, slope), jnp.int32)
    couples = (count - 1) // 2
    giver, taker = sizes[1:1 + 2 * couples:2], sizes[2:2 + 2 * couples:2]
    room = jnp.minimum(giver - 1, bound - taker)
    passed = jax.random.randint(jax.random.fold_in(key, 1), (couples,), 0, 1 << 20) % (room + 1)
    sizes = sizes.at[1:1 + 2 * couples:2].set(giver - passed).at[2:2 + 2 * couples:2].set(taker + passed)
    return sizes[jax.random.permutation(jax.random.fold_in(key, 2), count)]


def scatter_about(key, extent, width, limit, pieces=(), kind=jnp.bfloat16):
    loudness = shard_levels(key, extent, pieces, -0.22, 0.18) if pieces else 1.0
    drawn = jax.random.normal(key, extent, jnp.float32) * width * loudness
    return jnp.minimum(jnp.maximum(drawn, -limit), limit).astype(kind)


def setup_inputs(seed: int = 0) -> dict:
    arg_keys = jax.random.split(jax.random.key(seed), 13)
    incoming = scatter_about(arg_keys[0], (LAYERS, TOKENS, D), 1.0, 6.0, ((0, 8), (2, 64)))
    norm_gain = jnp.clip(1.0 + 0.1 * jax.random.normal(arg_keys[1], (LAYERS, D), jnp.float32), 0.5, 1.5).astype(jnp.bfloat16)
    query_weight = scatter_about(arg_keys[2], (LAYERS, D, HEADS * HD), D ** -0.5, 0.0625, ((0, 8), (1, 64)))
    query_scale = jnp.clip(jnp.exp(math.log(3.0) - 2.3025851 * jax.random.uniform(arg_keys[3], (LAYERS, D // BLK, HEADS * HD // BLK), jnp.float32) ** shard_levels(arg_keys[3], (LAYERS, D // BLK, HEADS * HD // BLK), ((0, 8), (1, 64)), -0.2, 0.2)), 0.3, 3.0)
    query_keep = draw_query_keep(jax.random.fold_in(arg_keys[12], 71), 0)
    kv_weight = scatter_about(arg_keys[5], (LAYERS, D, 2 * KV_HEADS * HD), D ** -0.5, 0.0625, ((0, 8), (1, 64)))
    kv_scale = jnp.clip(jnp.exp(math.log(3.0) - 2.3025851 * jax.random.uniform(arg_keys[6], (LAYERS, D // BLK, 2 * KV_HEADS * HD // BLK), jnp.float32) ** shard_levels(arg_keys[6], (LAYERS, D // BLK, 2 * KV_HEADS * HD // BLK), ((0, 8), (1, 64)), -0.2, 0.2)), 0.3, 3.0)
    kv_keep = draw_kv_keep(jax.random.fold_in(arg_keys[12], 71), 0)
    out_weight = scatter_about(arg_keys[8], (LAYERS, HEADS * HD, D), (HEADS * HD) ** -0.5, 0.0625, ((0, 8), (1, 64)))
    out_scale = jnp.clip(jnp.exp(math.log(3.0) - 2.3025851 * jax.random.uniform(arg_keys[9], (LAYERS, HEADS * HD // BLK, D // BLK), jnp.float32) ** shard_levels(arg_keys[9], (LAYERS, HEADS * HD // BLK, D // BLK), ((0, 8), (1, 64)), -0.2, 0.2)), 0.3, 3.0)
    out_keep = draw_out_keep(jax.random.fold_in(arg_keys[12], 71), 0)
    documents = jnp.searchsorted(jnp.cumsum(uneven(arg_keys[11], 4, TOKENS, SPAN, 0)), jnp.arange(TOKENS), side="right").astype(jnp.int32)
    return {"incoming": incoming, "norm_gain": norm_gain, "query_weight": query_weight, "query_scale": query_scale, "query_keep": query_keep, "kv_weight": kv_weight, "kv_scale": kv_scale, "kv_keep": kv_keep, "out_weight": out_weight, "out_scale": out_scale, "out_keep": out_keep, "documents": documents}


rope_base = 500000.0
epsilon = 1e-05

def dequant(weight, scale, keep):
    row_count, col_count = weight.shape
    factor = scale * keep.astype(jnp.float32)
    blocks = weight.astype(jnp.float32).reshape(row_count // BLK, BLK, col_count // BLK, BLK)
    blocks = blocks * factor[:, None, :, None]
    return blocks.reshape(row_count, col_count).astype(jnp.bfloat16)

def rotate(values, first_col):
    row_count, col_count = values.shape
    columns = first_col + 2 * jnp.arange(col_count // 2, dtype=jnp.int32)
    frequency = rope_base ** (-(columns % HD).astype(jnp.float32) / HD)
    angles = jnp.arange(row_count, dtype=jnp.float32)[:, None] * frequency[None, :]
    paired = values.reshape(row_count, col_count // 2, 2)
    even_part = paired[:, :, 0]
    odd_part = paired[:, :, 1]
    cosine = jnp.cos(angles)
    sine = jnp.sin(angles)
    turned = jnp.stack((even_part * cosine - odd_part * sine, even_part * sine + odd_part * cosine), axis=-1)
    return turned.reshape(row_count, col_count)

def reference(incoming, norm_gain, query_weight, query_scale, query_keep, kv_weight, kv_scale, kv_keep, out_weight, out_scale, out_keep, documents):
    kv_width = KV_HEADS * HD
    group_size = HEADS // KV_HEADS
    token_ids = jnp.arange(TOKENS, dtype=jnp.int32)
    allowed = (documents[:, None] == documents[None, :]) & (token_ids[:, None] >= token_ids[None, :])
    results = []
    for layer_index in range(LAYERS):
        activ = incoming[layer_index].astype(jnp.float32)
        mean_sq = lax.optimization_barrier(jnp.sum(activ * activ, axis=1, keepdims=True)) / D
        normed = (activ * lax.rsqrt(mean_sq + epsilon) * norm_gain[layer_index].astype(jnp.float32)).astype(jnp.bfloat16)
        q_eff = dequant(query_weight[layer_index], query_scale[layer_index], query_keep[layer_index])
        kv_eff = dequant(kv_weight[layer_index], kv_scale[layer_index], kv_keep[layer_index])
        o_eff = dequant(out_weight[layer_index], out_scale[layer_index], out_keep[layer_index])
        queries = rotate(jnp.dot(normed, q_eff, preferred_element_type=jnp.float32), 0).astype(jnp.bfloat16)
        keyval = jnp.dot(normed, kv_eff, preferred_element_type=jnp.float32)
        col_ids = jnp.arange(2 * kv_width, dtype=jnp.int32)
        keyval = jnp.where(col_ids[None, :] < kv_width, rotate(keyval, 0), keyval).astype(jnp.bfloat16)
        query_four = queries.astype(jnp.float32).reshape(TOKENS, KV_HEADS, group_size, HD)
        key_rows = keyval[:, :kv_width].astype(jnp.float32).reshape(TOKENS, KV_HEADS, HD)
        value_rows = keyval[:, kv_width:].astype(jnp.float32).reshape(TOKENS, KV_HEADS, HD)
        scores = jnp.einsum('tkgd,skd->kgts', query_four, key_rows) / jnp.sqrt(jnp.float32(HD))
        exp_scores = jnp.where(allowed[None, None], jnp.exp(scores), jnp.float32(0.0))
        probs = (exp_scores / lax.optimization_barrier(jnp.sum(exp_scores, axis=-1, keepdims=True))).astype(jnp.bfloat16)
        head_out = jnp.einsum('kgts,skd->tkgd', probs.astype(jnp.float32), value_rows)
        head_out = head_out.astype(jnp.bfloat16).reshape(TOKENS, HEADS * HD)
        mixed_sum = jnp.dot(head_out, o_eff, preferred_element_type=jnp.float32)
        results.append((activ + mixed_sum).astype(jnp.bfloat16))
    return jnp.roll(jnp.stack(results), 1, axis=0)
```

```python
import jax
import jax.numpy as jnp
from jax import lax
from jax.sharding import PartitionSpec as P

D = 8192
HEADS = 64
KV_HEADS = 8
HD = 128
BLK = 128


rope_base = 500000.0
epsilon = 1e-05


def passed_along(value, axis, steps):
    count = lax.axis_size(axis)
    pairs = [(source, (source + steps) % count) for source in range(count)]
    return lax.ppermute(value, axis, pairs)


def dequant(weight, scale, keep):
    row_count, col_count = weight.shape
    factor = scale * keep.astype(jnp.float32)
    blocks = weight.astype(jnp.float32).reshape(row_count // BLK, BLK, col_count // BLK, BLK)
    blocks = blocks * factor[:, None, :, None]
    return blocks.reshape(row_count, col_count).astype(jnp.bfloat16)


def rotate(values, first_col):
    row_count, col_count = values.shape
    columns = first_col + 2 * jnp.arange(col_count // 2, dtype=jnp.int32)
    frequency = rope_base ** (-(columns % HD).astype(jnp.float32) / HD)
    angles = jnp.arange(row_count, dtype=jnp.float32)[:, None] * frequency[None, :]
    paired = values.reshape(row_count, col_count // 2, 2)
    even_part = paired[:, :, 0]
    odd_part = paired[:, :, 1]
    cosine = jnp.cos(angles)
    sine = jnp.sin(angles)
    turned = jnp.stack(
        (even_part * cosine - odd_part * sine, even_part * sine + odd_part * cosine), axis=-1
    )
    return turned.reshape(row_count, col_count)


def gather_all(value, axis):
    count = lax.axis_size(axis)
    spread = jnp.broadcast_to(value[None], (count,) + value.shape)
    return lax.all_to_all(spread, axis, 0, 0, tiled=True)


def group_gather(value, axis, members):
    count = lax.axis_size(axis)
    own = lax.axis_index(axis)
    held = value[None]
    step = 1
    while step < members:
        pairs = [(source, source ^ step) for source in range(count)]
        other = lax.ppermute(held, axis, pairs)
        low = (own & step) == 0
        held = jnp.where(
            low, jnp.concatenate([held, other], 0), jnp.concatenate([other, held], 0)
        )
        step *= 2
    return held


def local(
    incoming,
    norm_gain,
    query_weight,
    query_scale,
    query_keep,
    kv_weight,
    kv_scale,
    kv_keep,
    out_weight,
    out_scale,
    out_keep,
    documents,
):
    tp = lax.axis_size("tp")
    own_index = lax.axis_index("tp")
    local_rows = incoming[0]
    tok_count, own_width = local_rows.shape
    kv_width = KV_HEADS * HD
    group_size = HEADS // KV_HEADS
    q_width = HEADS * HD // tp
    heads_here = q_width // HD
    members = group_size // heads_here
    chunk = HD // members

    q_eff = dequant(query_weight[0], query_scale[0], query_keep[0])
    q_columns = lax.all_to_all(q_eff, "tp", split_axis=1, concat_axis=0, tiled=True)
    kv_eff = dequant(kv_weight[0], kv_scale[0], kv_keep[0])
    kv_send = kv_eff.reshape(own_width, 2, KV_HEADS, members, chunk)
    kv_send = kv_send.transpose(2, 3, 0, 1, 4).reshape(tp, own_width, 2 * chunk)
    kv_columns = lax.all_to_all(kv_send, "tp", 0, 0, tiled=True)
    o_eff = dequant(out_weight[0], out_scale[0], out_keep[0])
    o_columns = lax.all_to_all(o_eff, "tp", split_axis=1, concat_axis=0, tiled=True)

    extended = jnp.concatenate([local_rows, norm_gain[0][None]], axis=0)
    gathered = gather_all(extended, "tp")
    activ_all = gathered[:, :tok_count, :].astype(jnp.float32)
    gain_all = gathered[:, tok_count, :].astype(jnp.float32)
    squares = jnp.sum(activ_all * activ_all, axis=(0, 2))
    scale_rows = lax.rsqrt(squares / D + epsilon)
    normed_all = (activ_all * scale_rows[None, :, None] * gain_all[:, None, :]).astype(jnp.bfloat16)
    normed_all = normed_all.transpose(1, 0, 2).reshape(tok_count, D)

    queries = jnp.dot(normed_all, q_columns, preferred_element_type=jnp.float32)
    queries = rotate(queries, own_index * q_width).astype(jnp.bfloat16)

    kv_part = jnp.dot(
        normed_all, kv_columns.reshape(D, 2 * chunk), preferred_element_type=jnp.float32
    )
    member = own_index % members
    key_part = rotate(kv_part[:, :chunk], member * chunk)
    kv_part = jnp.concatenate([key_part, kv_part[:, chunk:]], axis=1).astype(jnp.bfloat16)
    kv_group = group_gather(kv_part, "tp", members)
    key_rows = kv_group[:, :, :chunk].transpose(1, 0, 2).reshape(tok_count, HD)
    value_rows = kv_group[:, :, chunk:].transpose(1, 0, 2).reshape(tok_count, HD)

    token_ids = jnp.arange(tok_count, dtype=jnp.int32)
    allowed = (documents[:, None] == documents[None, :]) & (
        token_ids[:, None] >= token_ids[None, :]
    )
    query_three = queries.reshape(tok_count, heads_here, HD)
    scores = jnp.einsum(
        "thd,sd->hts", query_three, key_rows, preferred_element_type=jnp.float32
    ) / jnp.sqrt(jnp.float32(HD))
    exp_scores = jnp.where(allowed[None], jnp.exp(scores), jnp.float32(0.0))
    probs = (exp_scores / jnp.sum(exp_scores, axis=-1, keepdims=True)).astype(jnp.bfloat16)
    head_out = jnp.einsum("hts,sd->thd", probs, value_rows, preferred_element_type=jnp.float32)
    head_out = head_out.astype(jnp.bfloat16).reshape(tok_count, q_width)

    heads_all = gather_all(head_out, "tp").transpose(1, 0, 2).reshape(tok_count, tp * q_width)
    mixed_sum = jnp.dot(heads_all, o_columns, preferred_element_type=jnp.float32)
    layer_out = (local_rows.astype(jnp.float32) + mixed_sum).astype(jnp.bfloat16)
    received = passed_along(layer_out, "section", 1)
    return received[None]


def solution(mesh):
    placed = (
        P("section", None, "tp"),
        P("section", "tp"),
        P("section", "tp", None),
        P("section", "tp", None),
        P("section", "tp", None),
        P("section", "tp", None),
        P("section", "tp", None),
        P("section", "tp", None),
        P("section", "tp", None),
        P("section", "tp", None),
        P("section", "tp", None),
        P(),
    )
    return jax.shard_map(
        local, mesh=mesh, in_specs=placed, out_specs=P("section", None, "tp"), check_vma=False
    )
```

```python
import jax
import jax.numpy as jnp
from jax import lax
from jax.sharding import Mesh
from jax.sharding import PartitionSpec as P

D = 8192
HEADS = 64
KV_HEADS = 8
HD = 128
BLK = 128


rope_base = 500000.0
epsilon = 1e-05


def passed_along(value, axis, steps):
    count = lax.axis_size(axis)
    pairs = [(source, (source + steps) % count) for source in range(count)]
    return lax.ppermute(value, axis, pairs)


def dequant(weight, scale, keep):
    row_count, col_count = weight.shape
    factor = scale * keep.astype(jnp.float32)
    blocks = weight.astype(jnp.float32).reshape(row_count // BLK, BLK, col_count // BLK, BLK)
    blocks = blocks * factor[:, None, :, None]
    return blocks.reshape(row_count, col_count).astype(jnp.bfloat16)


def rotate(values, first_col):
    row_count, col_count = values.shape
    columns = first_col + 2 * jnp.arange(col_count // 2, dtype=jnp.int32)
    frequency = rope_base ** (-(columns % HD).astype(jnp.float32) / HD)
    angles = jnp.arange(row_count, dtype=jnp.float32)[:, None] * frequency[None, :]
    paired = values.reshape(row_count, col_count // 2, 2)
    even_part = paired[:, :, 0]
    odd_part = paired[:, :, 1]
    cosine = jnp.cos(angles)
    sine = jnp.sin(angles)
    turned = jnp.stack(
        (even_part * cosine - odd_part * sine, even_part * sine + odd_part * cosine), axis=-1
    )
    return turned.reshape(row_count, col_count)


def gather_all(value, axes):
    held = value[None]
    for axis in reversed(axes):
        count = lax.axis_size(axis)
        spread = jnp.broadcast_to(held[None], (count,) + held.shape)
        held = lax.all_to_all(spread, axis, 0, 0, tiled=True)
        held = held.reshape((-1,) + value.shape)
    return held


def group_gather(value, axis, members):
    count = lax.axis_size(axis)
    own = lax.axis_index(axis)
    held = value[None]
    step = 1
    while step < members:
        pairs = [(source, source ^ step) for source in range(count)]
        other = lax.ppermute(held, axis, pairs)
        low = (own & step) == 0
        held = jnp.where(
            low, jnp.concatenate([held, other], 0), jnp.concatenate([other, held], 0)
        )
        step *= 2
    return held


def local(
    incoming,
    norm_gain,
    query_weight,
    query_scale,
    query_keep,
    kv_weight,
    kv_scale,
    kv_keep,
    out_weight,
    out_scale,
    out_keep,
    documents,
):
    tp = lax.axis_size(TP_AXES)
    own_index = lax.axis_index(TP_AXES)
    local_rows = incoming[0]
    tok_count, own_width = local_rows.shape
    kv_width = KV_HEADS * HD
    group_size = HEADS // KV_HEADS
    q_width = HEADS * HD // tp
    heads_here = q_width // HD
    members = group_size // heads_here
    chunk = HD // members

    q_eff = dequant(query_weight[0], query_scale[0], query_keep[0])
    q_columns = lax.all_to_all(q_eff, TP_AXES, split_axis=1, concat_axis=0, tiled=True)
    kv_eff = dequant(kv_weight[0], kv_scale[0], kv_keep[0])
    kv_send = kv_eff.reshape(own_width, 2, KV_HEADS, members, chunk)
    kv_send = kv_send.transpose(2, 3, 0, 1, 4).reshape(tp, own_width, 2 * chunk)
    kv_columns = lax.all_to_all(kv_send, TP_AXES, 0, 0, tiled=True)
    o_eff = dequant(out_weight[0], out_scale[0], out_keep[0])
    o_columns = lax.all_to_all(o_eff, TP_AXES, split_axis=1, concat_axis=0, tiled=True)

    extended = jnp.concatenate([local_rows, norm_gain[0][None]], axis=0)
    gathered = gather_all(extended, TP_AXES)
    activ_all = gathered[:, :tok_count, :].astype(jnp.float32)
    gain_all = gathered[:, tok_count, :].astype(jnp.float32)
    squares = jnp.sum(activ_all * activ_all, axis=(0, 2))
    scale_rows = lax.rsqrt(squares / D + epsilon)
    normed_all = (activ_all * scale_rows[None, :, None] * gain_all[:, None, :]).astype(jnp.bfloat16)
    normed_all = normed_all.transpose(1, 0, 2).reshape(tok_count, D)

    queries = jnp.dot(normed_all, q_columns, preferred_element_type=jnp.float32)
    queries = rotate(queries, own_index * q_width).astype(jnp.bfloat16)

    kv_part = jnp.dot(
        normed_all, kv_columns.reshape(D, 2 * chunk), preferred_element_type=jnp.float32
    )
    member = own_index % members
    key_part = rotate(kv_part[:, :chunk], member * chunk)
    kv_part = jnp.concatenate([key_part, kv_part[:, chunk:]], axis=1).astype(jnp.bfloat16)
    kv_group = group_gather(kv_part, TP_AXES, members)
    key_rows = kv_group[:, :, :chunk].transpose(1, 0, 2).reshape(tok_count, HD)
    value_rows = kv_group[:, :, chunk:].transpose(1, 0, 2).reshape(tok_count, HD)

    token_ids = jnp.arange(tok_count, dtype=jnp.int32)
    allowed = (documents[:, None] == documents[None, :]) & (
        token_ids[:, None] >= token_ids[None, :]
    )
    query_three = queries.reshape(tok_count, heads_here, HD)
    scores = jnp.einsum(
        "thd,sd->hts", query_three, key_rows, preferred_element_type=jnp.float32
    ) / jnp.sqrt(jnp.float32(HD))
    exp_scores = jnp.where(allowed[None], jnp.exp(scores), jnp.float32(0.0))
    probs = (exp_scores / jnp.sum(exp_scores, axis=-1, keepdims=True)).astype(jnp.bfloat16)
    head_out = jnp.einsum("hts,sd->thd", probs, value_rows, preferred_element_type=jnp.float32)
    head_out = head_out.astype(jnp.bfloat16).reshape(tok_count, q_width)

    heads_all = gather_all(head_out, TP_AXES).transpose(1, 0, 2).reshape(tok_count, tp * q_width)
    mixed_sum = jnp.dot(heads_all, o_columns, preferred_element_type=jnp.float32)
    layer_out = (local_rows.astype(jnp.float32) + mixed_sum).astype(jnp.bfloat16)
    received = passed_along(layer_out, "section", 1)
    return received[None]


TP_AXES = ("tp_x", "tp_z", "tp_y")


def solution(mesh):
    devices = mesh.devices.reshape(mesh.shape["section"], 4, 4, -1)
    mesh = Mesh(devices, ("section",) + TP_AXES)
    tp = TP_AXES
    placed = (
        P("section", None, tp),
        P("section", tp),
        P("section", tp, None),
        P("section", tp, None),
        P("section", tp, None),
        P("section", tp, None),
        P("section", tp, None),
        P("section", tp, None),
        P("section", tp, None),
        P("section", tp, None),
        P("section", tp, None),
        P(),
    )
    return jax.shard_map(
        local, mesh=mesh, in_specs=placed, out_specs=P("section", None, tp), check_vma=False
    )
```

```python
import jax
import jax.numpy as jnp
from jax import lax
from jax.sharding import Mesh
from jax.sharding import PartitionSpec as P

D = 8192
HEADS = 64
KV_HEADS = 8
HD = 128
BLK = 128


rope_base = 500000.0
epsilon = 1e-05


def passed_along(value, axis, steps):
    count = lax.axis_size(axis)
    pairs = [(source, (source + steps) % count) for source in range(count)]
    return lax.ppermute(value, axis, pairs)


def dequant(weight, scale, keep):
    row_count, col_count = weight.shape
    factor = scale * keep.astype(jnp.float32)
    blocks = weight.astype(jnp.float32).reshape(row_count // BLK, BLK, col_count // BLK, BLK)
    blocks = blocks * factor[:, None, :, None]
    return blocks.reshape(row_count, col_count).astype(jnp.bfloat16)


def rotate(values, first_col):
    row_count, col_count = values.shape
    columns = first_col + 2 * jnp.arange(col_count // 2, dtype=jnp.int32)
    frequency = rope_base ** (-(columns % HD).astype(jnp.float32) / HD)
    angles = jnp.arange(row_count, dtype=jnp.float32)[:, None] * frequency[None, :]
    paired = values.reshape(row_count, col_count // 2, 2)
    even_part = paired[:, :, 0]
    odd_part = paired[:, :, 1]
    cosine = jnp.cos(angles)
    sine = jnp.sin(angles)
    turned = jnp.stack(
        (even_part * cosine - odd_part * sine, even_part * sine + odd_part * cosine), axis=-1
    )
    return turned.reshape(row_count, col_count)


def gather_all(value, axes):
    held = value[None]
    for axis in reversed(axes):
        count = lax.axis_size(axis)
        spread = jnp.broadcast_to(held[None], (count,) + held.shape)
        held = lax.all_to_all(spread, axis, 0, 0, tiled=True)
        held = held.reshape((-1,) + value.shape)
    return held


def group_gather(value, axis, members):
    count = lax.axis_size(axis)
    own = lax.axis_index(axis)
    held = value[None]
    step = 1
    while step < members:
        pairs = [(source, source ^ step) for source in range(count)]
        other = lax.ppermute(held, axis, pairs)
        low = (own & step) == 0
        held = jnp.where(
            low, jnp.concatenate([held, other], 0), jnp.concatenate([other, held], 0)
        )
        step *= 2
    return held


def local(
    incoming,
    norm_gain,
    query_weight,
    query_scale,
    query_keep,
    kv_weight,
    kv_scale,
    kv_keep,
    out_weight,
    out_scale,
    out_keep,
    documents,
):
    tp = lax.axis_size(TP_AXES)
    own_index = lax.axis_index(TP_AXES)
    planes = lax.axis_size(CROSS)
    plane = lax.axis_size(PLANE)
    local_rows = incoming[0]
    tok_count, own_width = local_rows.shape
    group_size = HEADS // KV_HEADS
    q_width = HEADS * HD // tp
    heads_here = q_width // HD
    members = group_size // heads_here
    chunk = HD // members
    halves = plane // members

    q_eff = dequant(query_weight[0], query_scale[0], query_keep[0])
    q_send = q_eff.reshape(own_width, planes, plane, q_width).transpose(2, 0, 1, 3)
    q_rows = lax.all_to_all(q_send, PLANE, 0, 0, tiled=True)
    q_rows = q_rows.reshape(plane * own_width, planes * q_width)
    kv_eff = dequant(kv_weight[0], kv_scale[0], kv_keep[0])
    kv_send = kv_eff.reshape(own_width, 2, planes, halves, members, chunk)
    kv_send = kv_send.transpose(3, 4, 0, 2, 1, 5).reshape(plane, own_width, planes * 2 * chunk)
    kv_rows = lax.all_to_all(kv_send, PLANE, 0, 0, tiled=True)
    kv_rows = kv_rows.reshape(plane * own_width, planes * 2 * chunk)
    o_eff = dequant(out_weight[0], out_scale[0], out_keep[0])
    o_send = o_eff.reshape(q_width, planes, plane, own_width).transpose(2, 0, 1, 3)
    o_rows = lax.all_to_all(o_send, PLANE, 0, 0, tiled=True)
    o_rows = o_rows.reshape(plane * q_width, planes * own_width)

    extended = jnp.concatenate([local_rows, norm_gain[0][None]], axis=0)
    gathered = gather_all(extended, PLANE)
    activ_pl = gathered[:, :tok_count, :].astype(jnp.float32)
    gain_pl = gathered[:, tok_count, :].astype(jnp.float32)
    partial_sq = jnp.sum(activ_pl * activ_pl, axis=(0, 2))
    squares = jnp.sum(gather_all(partial_sq, (CROSS,)), axis=0)
    scale_rows = lax.rsqrt(squares / D + epsilon)
    normed_pl = (activ_pl * scale_rows[None, :, None] * gain_pl[:, None, :]).astype(jnp.bfloat16)
    normed_pl = normed_pl.transpose(1, 0, 2).reshape(tok_count, plane * own_width)

    q_part = jnp.dot(normed_pl, q_rows, preferred_element_type=jnp.float32)
    kv_part = jnp.dot(normed_pl, kv_rows, preferred_element_type=jnp.float32)
    packed = jnp.concatenate(
        [q_part.reshape(tok_count, planes, q_width), kv_part.reshape(tok_count, planes, 2 * chunk)],
        axis=2,
    ).transpose(1, 0, 2)
    summed = jnp.sum(lax.all_to_all(packed, CROSS, 0, 0, tiled=True), axis=0)

    queries = rotate(summed[:, :q_width], own_index * q_width).astype(jnp.bfloat16)
    member = own_index % members
    key_part = rotate(summed[:, q_width : q_width + chunk], member * chunk)
    kv_part = jnp.concatenate([key_part, summed[:, q_width + chunk :]], axis=1).astype(jnp.bfloat16)
    kv_group = group_gather(kv_part, TP_AXES, members)
    key_rows = kv_group[:, :, :chunk].transpose(1, 0, 2).reshape(tok_count, HD)
    value_rows = kv_group[:, :, chunk:].transpose(1, 0, 2).reshape(tok_count, HD)

    token_ids = jnp.arange(tok_count, dtype=jnp.int32)
    allowed = (documents[:, None] == documents[None, :]) & (
        token_ids[:, None] >= token_ids[None, :]
    )
    query_three = queries.reshape(tok_count, heads_here, HD)
    scores = jnp.einsum(
        "thd,sd->hts", query_three, key_rows, preferred_element_type=jnp.float32
    ) / jnp.sqrt(jnp.float32(HD))
    exp_scores = jnp.where(allowed[None], jnp.exp(scores), jnp.float32(0.0))
    probs = (exp_scores / jnp.sum(exp_scores, axis=-1, keepdims=True)).astype(jnp.bfloat16)
    head_out = jnp.einsum("hts,sd->thd", probs, value_rows, preferred_element_type=jnp.float32)
    head_out = head_out.astype(jnp.bfloat16).reshape(tok_count, q_width)

    heads_pl = gather_all(head_out, PLANE).transpose(1, 0, 2).reshape(tok_count, plane * q_width)
    out_part = jnp.dot(heads_pl, o_rows, preferred_element_type=jnp.float32)
    out_part = out_part.reshape(tok_count, planes, own_width).transpose(1, 0, 2)
    mixed_sum = jnp.sum(lax.all_to_all(out_part, CROSS, 0, 0, tiled=True), axis=0)
    layer_out = (local_rows.astype(jnp.float32) + mixed_sum).astype(jnp.bfloat16)
    received = passed_along(layer_out, "section", 1)
    return received[None]


TP_AXES = ("tp_x", "tp_z", "tp_y")
CROSS = "tp_x"
PLANE = ("tp_z", "tp_y")


def solution(mesh):
    devices = mesh.devices.reshape(mesh.shape["section"], 4, 4, -1)
    mesh = Mesh(devices, ("section",) + TP_AXES)
    tp = TP_AXES
    placed = (
        P("section", None, tp),
        P("section", tp),
        P("section", tp, None),
        P("section", tp, None),
        P("section", tp, None),
        P("section", tp, None),
        P("section", tp, None),
        P("section", tp, None),
        P("section", tp, None),
        P("section", tp, None),
        P("section", tp, None),
        P(),
    )
    return jax.shard_map(
        local, mesh=mesh, in_specs=placed, out_specs=P("section", None, tp), check_vma=False
    )
```

```python
import jax
import jax.numpy as jnp
from jax import lax
from jax.sharding import Mesh
from jax.sharding import PartitionSpec as P

D = 8192
HEADS = 64
KV_HEADS = 8
HD = 128
BLK = 128


rope_base = 500000.0
epsilon = 1e-05


def passed_along(value, axis, steps):
    count = lax.axis_size(axis)
    pairs = [(source, (source + steps) % count) for source in range(count)]
    return lax.ppermute(value, axis, pairs)


def dequant(weight, scale, keep):
    row_count, col_count = weight.shape
    factor = scale * keep.astype(jnp.float32)
    blocks = weight.astype(jnp.float32).reshape(row_count // BLK, BLK, col_count // BLK, BLK)
    blocks = blocks * factor[:, None, :, None]
    return blocks.reshape(row_count, col_count).astype(jnp.bfloat16)


def rotate(values, first_col):
    row_count, col_count = values.shape
    columns = first_col + 2 * jnp.arange(col_count // 2, dtype=jnp.int32)
    frequency = rope_base ** (-(columns % HD).astype(jnp.float32) / HD)
    angles = jnp.arange(row_count, dtype=jnp.float32)[:, None] * frequency[None, :]
    paired = values.reshape(row_count, col_count // 2, 2)
    even_part = paired[:, :, 0]
    odd_part = paired[:, :, 1]
    cosine = jnp.cos(angles)
    sine = jnp.sin(angles)
    turned = jnp.stack(
        (even_part * cosine - odd_part * sine, even_part * sine + odd_part * cosine), axis=-1
    )
    return turned.reshape(row_count, col_count)


def gather_all(value, axes):
    held = value[None]
    for axis in reversed(axes):
        count = lax.axis_size(axis)
        spread = jnp.broadcast_to(held[None], (count,) + held.shape)
        held = lax.all_to_all(spread, axis, 0, 0, tiled=True)
        held = held.reshape((-1,) + value.shape)
    return held


def group_gather(value, axis, members):
    count = lax.axis_size(axis)
    own = lax.axis_index(axis)
    held = value[None]
    step = 1
    while step < members:
        pairs = [(source, source ^ step) for source in range(count)]
        other = lax.ppermute(held, axis, pairs)
        low = (own & step) == 0
        held = jnp.where(
            low, jnp.concatenate([held, other], 0), jnp.concatenate([other, held], 0)
        )
        step *= 2
    return held


def local(
    incoming,
    norm_gain,
    query_weight,
    query_scale,
    query_keep,
    kv_weight,
    kv_scale,
    kv_keep,
    out_weight,
    out_scale,
    out_keep,
    documents,
):
    tp = lax.axis_size(TP_AXES)
    own_index = lax.axis_index(TP_AXES)
    planes = lax.axis_size(CROSS)
    plane = lax.axis_size(PLANE)
    local_rows = incoming[0]
    tok_count, own_width = local_rows.shape
    group_size = HEADS // KV_HEADS
    q_width = HEADS * HD // tp
    heads_here = q_width // HD
    members = group_size // heads_here
    chunk = HD // members
    halves = plane // members

    q_eff = dequant(query_weight[0], query_scale[0], query_keep[0])
    q_send = q_eff.reshape(own_width, planes, plane, q_width).transpose(2, 0, 1, 3)
    q_rows = lax.all_to_all(q_send, PLANE, 0, 0, tiled=True)
    q_rows = q_rows.reshape(plane * own_width, planes * q_width)
    kv_eff = dequant(kv_weight[0], kv_scale[0], kv_keep[0])
    kv_send = kv_eff.reshape(own_width, 2, planes, halves, members, chunk)
    kv_send = kv_send.transpose(3, 4, 0, 2, 1, 5).reshape(plane, own_width, planes * 2 * chunk)
    kv_rows = lax.all_to_all(kv_send, PLANE, 0, 0, tiled=True)
    kv_rows = kv_rows.reshape(plane * own_width, planes * 2 * chunk)
    o_eff = dequant(out_weight[0], out_scale[0], out_keep[0])
    o_send = o_eff.reshape(q_width, planes, plane, own_width).transpose(2, 0, 1, 3)
    o_rows = lax.all_to_all(o_send, PLANE, 0, 0, tiled=True)
    o_rows = o_rows.reshape(plane * q_width, planes * own_width)

    extended = jnp.concatenate([local_rows, norm_gain[0][None]], axis=0)
    gathered = gather_all(extended, PLANE)
    activ_pl = gathered[:, :tok_count, :].astype(jnp.float32)
    gain_pl = gathered[:, tok_count, :].astype(jnp.float32)
    partial_sq = jnp.sum(activ_pl * activ_pl, axis=(0, 2))
    squares = jnp.sum(gather_all(partial_sq, (CROSS,)), axis=0)
    scale_rows = lax.rsqrt(squares / D + epsilon)
    normed_pl = (activ_pl * scale_rows[None, :, None] * gain_pl[:, None, :]).astype(jnp.bfloat16)
    normed_pl = normed_pl.transpose(1, 0, 2).reshape(tok_count, plane * own_width)

    q_part = jnp.dot(normed_pl, q_rows, preferred_element_type=jnp.float32)
    kv_part = jnp.dot(normed_pl, kv_rows, preferred_element_type=jnp.float32)
    packed = jnp.concatenate(
        [q_part.reshape(tok_count, planes, q_width), kv_part.reshape(tok_count, planes, 2 * chunk)],
        axis=2,
    ).transpose(1, 0, 2)
    summed = jnp.sum(lax.all_to_all(packed, CROSS, 0, 0, tiled=True), axis=0)

    queries = rotate(summed[:, :q_width], own_index * q_width).astype(jnp.bfloat16)
    member = own_index % members
    key_part = rotate(summed[:, q_width : q_width + chunk], member * chunk)
    kv_part = jnp.concatenate([key_part, summed[:, q_width + chunk :]], axis=1).astype(jnp.bfloat16)
    plane_all = gather_all(kv_part, PLANE)
    first = (lax.axis_index(PLANE) // members) * members
    kv_group = lax.dynamic_slice_in_dim(plane_all, first, members, 0)
    key_rows = kv_group[:, :, :chunk].transpose(1, 0, 2).reshape(tok_count, HD)
    value_rows = kv_group[:, :, chunk:].transpose(1, 0, 2).reshape(tok_count, HD)

    token_ids = jnp.arange(tok_count, dtype=jnp.int32)
    allowed = (documents[:, None] == documents[None, :]) & (
        token_ids[:, None] >= token_ids[None, :]
    )
    query_three = queries.reshape(tok_count, heads_here, HD)
    scores = jnp.einsum(
        "thd,sd->hts", query_three, key_rows, preferred_element_type=jnp.float32
    ) / jnp.sqrt(jnp.float32(HD))
    exp_scores = jnp.where(allowed[None], jnp.exp(scores), jnp.float32(0.0))
    probs = (exp_scores / jnp.sum(exp_scores, axis=-1, keepdims=True)).astype(jnp.bfloat16)
    head_out = jnp.einsum("hts,sd->thd", probs, value_rows, preferred_element_type=jnp.float32)
    head_out = head_out.astype(jnp.bfloat16).reshape(tok_count, q_width)

    heads_pl = gather_all(head_out, PLANE).transpose(1, 0, 2).reshape(tok_count, plane * q_width)
    out_part = jnp.dot(heads_pl, o_rows, preferred_element_type=jnp.float32)
    out_part = out_part.reshape(tok_count, planes, own_width).transpose(1, 0, 2)
    mixed_sum = jnp.sum(lax.all_to_all(out_part, CROSS, 0, 0, tiled=True), axis=0)
    layer_out = (local_rows.astype(jnp.float32) + mixed_sum).astype(jnp.bfloat16)
    received = passed_along(layer_out, "section", 1)
    return received[None]


TP_AXES = ("tp_x", "tp_z", "tp_y")
CROSS = "tp_x"
PLANE = ("tp_z", "tp_y")


def solution(mesh):
    devices = mesh.devices.reshape(mesh.shape["section"], 4, 4, -1)
    mesh = Mesh(devices, ("section",) + TP_AXES)
    tp = TP_AXES
    placed = (
        P("section", None, tp),
        P("section", tp),
        P("section", tp, None),
        P("section", tp, None),
        P("section", tp, None),
        P("section", tp, None),
        P("section", tp, None),
        P("section", tp, None),
        P("section", tp, None),
        P("section", tp, None),
        P("section", tp, None),
        P(),
    )
    return jax.shard_map(
        local, mesh=mesh, in_specs=placed, out_specs=P("section", None, tp), check_vma=False
    )
```

```python
import jax
import jax.numpy as jnp
from jax import lax
from jax.sharding import Mesh
from jax.sharding import PartitionSpec as P

D = 8192
HEADS = 64
KV_HEADS = 8
HD = 128
BLK = 128


rope_base = 500000.0
epsilon = 1e-05


def passed_along(value, axis, steps):
    count = lax.axis_size(axis)
    pairs = [(source, (source + steps) % count) for source in range(count)]
    return lax.ppermute(value, axis, pairs)


def dequant(weight, scale, keep):
    row_count, col_count = weight.shape
    factor = scale * keep.astype(jnp.float32)
    blocks = weight.astype(jnp.float32).reshape(row_count // BLK, BLK, col_count // BLK, BLK)
    blocks = blocks * factor[:, None, :, None]
    return blocks.reshape(row_count, col_count).astype(jnp.bfloat16)


def rotate(values, first_col):
    row_count, col_count = values.shape
    columns = first_col + 2 * jnp.arange(col_count // 2, dtype=jnp.int32)
    frequency = rope_base ** (-(columns % HD).astype(jnp.float32) / HD)
    angles = jnp.arange(row_count, dtype=jnp.float32)[:, None] * frequency[None, :]
    paired = values.reshape(row_count, col_count // 2, 2)
    even_part = paired[:, :, 0]
    odd_part = paired[:, :, 1]
    cosine = jnp.cos(angles)
    sine = jnp.sin(angles)
    turned = jnp.stack(
        (even_part * cosine - odd_part * sine, even_part * sine + odd_part * cosine), axis=-1
    )
    return turned.reshape(row_count, col_count)


def gather_all(value, axes):
    held = value[None]
    for axis in reversed(axes):
        count = lax.axis_size(axis)
        spread = jnp.broadcast_to(held[None], (count,) + held.shape)
        held = lax.all_to_all(spread, axis, 0, 0, tiled=True)
        held = held.reshape((-1,) + value.shape)
    return held


def group_gather(value, axis, members):
    count = lax.axis_size(axis)
    own = lax.axis_index(axis)
    held = value[None]
    step = 1
    while step < members:
        pairs = [(source, source ^ step) for source in range(count)]
        other = lax.ppermute(held, axis, pairs)
        low = (own & step) == 0
        held = jnp.where(
            low, jnp.concatenate([held, other], 0), jnp.concatenate([other, held], 0)
        )
        step *= 2
    return held


def local(
    incoming,
    norm_gain,
    query_weight,
    query_scale,
    query_keep,
    kv_weight,
    kv_scale,
    kv_keep,
    out_weight,
    out_scale,
    out_keep,
    documents,
):
    tp = lax.axis_size(TP_AXES)
    own_index = lax.axis_index(TP_AXES)
    planes = lax.axis_size(CROSS)
    plane = lax.axis_size(PLANE)
    local_rows = incoming[0]
    tok_count, own_width = local_rows.shape
    group_size = HEADS // KV_HEADS
    q_width = HEADS * HD // tp
    heads_here = q_width // HD
    members = group_size // heads_here
    chunk = HD // members
    halves = plane // members

    q_eff = dequant(query_weight[0], query_scale[0], query_keep[0])
    q_send = q_eff.reshape(own_width, planes, plane, q_width).transpose(2, 0, 1, 3)
    q_send = q_send.reshape(plane, own_width, planes * q_width)
    kv_eff = dequant(kv_weight[0], kv_scale[0], kv_keep[0])
    kv_send = kv_eff.reshape(own_width, 2, planes, halves, members, chunk)
    kv_send = kv_send.transpose(3, 4, 0, 2, 1, 5).reshape(plane, own_width, planes * 2 * chunk)
    both = jnp.concatenate([q_send, kv_send], axis=2)
    both = lax.all_to_all(both, PLANE, 0, 0, tiled=True).reshape(plane * own_width, -1)
    q_rows = both[:, : planes * q_width]
    kv_rows = both[:, planes * q_width :]
    o_eff = dequant(out_weight[0], out_scale[0], out_keep[0])
    o_send = o_eff.reshape(q_width, planes, plane, own_width).transpose(2, 0, 1, 3)
    o_rows = lax.all_to_all(o_send, PLANE, 0, 0, tiled=True)
    o_rows = o_rows.reshape(plane * q_width, planes * own_width)

    extended = jnp.concatenate([local_rows, norm_gain[0][None]], axis=0)
    gathered = gather_all(extended, PLANE)
    activ_pl = gathered[:, :tok_count, :].astype(jnp.float32)
    gain_pl = gathered[:, tok_count, :].astype(jnp.float32)
    partial_sq = jnp.sum(activ_pl * activ_pl, axis=(0, 2))
    squares = jnp.sum(gather_all(partial_sq, (CROSS,)), axis=0)
    scale_rows = lax.rsqrt(squares / D + epsilon)
    normed_pl = (activ_pl * scale_rows[None, :, None] * gain_pl[:, None, :]).astype(jnp.bfloat16)
    normed_pl = normed_pl.transpose(1, 0, 2).reshape(tok_count, plane * own_width)

    q_part = jnp.dot(normed_pl, q_rows, preferred_element_type=jnp.float32)
    kv_part = jnp.dot(normed_pl, kv_rows, preferred_element_type=jnp.float32)
    packed = jnp.concatenate(
        [q_part.reshape(tok_count, planes, q_width), kv_part.reshape(tok_count, planes, 2 * chunk)],
        axis=2,
    ).transpose(1, 0, 2)
    summed = jnp.sum(lax.all_to_all(packed, CROSS, 0, 0, tiled=True), axis=0)

    queries = rotate(summed[:, :q_width], own_index * q_width).astype(jnp.bfloat16)
    member = own_index % members
    key_part = rotate(summed[:, q_width : q_width + chunk], member * chunk)
    kv_part = jnp.concatenate([key_part, summed[:, q_width + chunk :]], axis=1).astype(jnp.bfloat16)
    kv_group = group_gather(kv_part, TP_AXES, members)
    key_rows = kv_group[:, :, :chunk].transpose(1, 0, 2).reshape(tok_count, HD)
    value_rows = kv_group[:, :, chunk:].transpose(1, 0, 2).reshape(tok_count, HD)

    token_ids = jnp.arange(tok_count, dtype=jnp.int32)
    allowed = (documents[:, None] == documents[None, :]) & (
        token_ids[:, None] >= token_ids[None, :]
    )
    query_three = queries.reshape(tok_count, heads_here, HD)
    scores = jnp.einsum(
        "thd,sd->hts", query_three, key_rows, preferred_element_type=jnp.float32
    ) / jnp.sqrt(jnp.float32(HD))
    exp_scores = jnp.where(allowed[None], jnp.exp(scores), jnp.float32(0.0))
    probs = (exp_scores / jnp.sum(exp_scores, axis=-1, keepdims=True)).astype(jnp.bfloat16)
    head_out = jnp.einsum("hts,sd->thd", probs, value_rows, preferred_element_type=jnp.float32)
    head_out = head_out.astype(jnp.bfloat16).reshape(tok_count, q_width)

    heads_pl = gather_all(head_out, PLANE).transpose(1, 0, 2).reshape(tok_count, plane * q_width)
    out_part = jnp.dot(heads_pl, o_rows, preferred_element_type=jnp.float32)
    out_part = out_part.reshape(tok_count, planes, own_width).transpose(1, 0, 2)
    mixed_sum = jnp.sum(lax.all_to_all(out_part, CROSS, 0, 0, tiled=True), axis=0)
    layer_out = (local_rows.astype(jnp.float32) + mixed_sum).astype(jnp.bfloat16)
    received = passed_along(layer_out, "section", 1)
    return received[None]


TP_AXES = ("tp_x", "tp_z", "tp_y")
CROSS = "tp_x"
PLANE = ("tp_z", "tp_y")


def solution(mesh):
    devices = mesh.devices.reshape(mesh.shape["section"], 4, 4, -1)
    mesh = Mesh(devices, ("section",) + TP_AXES)
    tp = TP_AXES
    placed = (
        P("section", None, tp),
        P("section", tp),
        P("section", tp, None),
        P("section", tp, None),
        P("section", tp, None),
        P("section", tp, None),
        P("section", tp, None),
        P("section", tp, None),
        P("section", tp, None),
        P("section", tp, None),
        P("section", tp, None),
        P(),
    )
    return jax.shard_map(
        local, mesh=mesh, in_specs=placed, out_specs=P("section", None, tp), check_vma=False
    )
```

```python
import jax
import jax.numpy as jnp
from jax import lax
from jax.sharding import Mesh
from jax.sharding import PartitionSpec as P

D = 8192
HEADS = 64
KV_HEADS = 8
HD = 128
BLK = 128


rope_base = 500000.0
epsilon = 1e-05


def passed_along(value, axis, steps):
    count = lax.axis_size(axis)
    pairs = [(source, (source + steps) % count) for source in range(count)]
    return lax.ppermute(value, axis, pairs)


def dequant(weight, scale, keep):
    row_count, col_count = weight.shape
    factor = scale * keep.astype(jnp.float32)
    blocks = weight.astype(jnp.float32).reshape(row_count // BLK, BLK, col_count // BLK, BLK)
    blocks = blocks * factor[:, None, :, None]
    return blocks.reshape(row_count, col_count).astype(jnp.bfloat16)


def rotate(values, first_col):
    row_count, col_count = values.shape
    columns = first_col + 2 * jnp.arange(col_count // 2, dtype=jnp.int32)
    frequency = rope_base ** (-(columns % HD).astype(jnp.float32) / HD)
    angles = jnp.arange(row_count, dtype=jnp.float32)[:, None] * frequency[None, :]
    paired = values.reshape(row_count, col_count // 2, 2)
    even_part = paired[:, :, 0]
    odd_part = paired[:, :, 1]
    cosine = jnp.cos(angles)
    sine = jnp.sin(angles)
    turned = jnp.stack(
        (even_part * cosine - odd_part * sine, even_part * sine + odd_part * cosine), axis=-1
    )
    return turned.reshape(row_count, col_count)


def gather_all(value, axes):
    held = value[None]
    for axis in reversed(axes):
        count = lax.axis_size(axis)
        spread = jnp.broadcast_to(held[None], (count,) + held.shape)
        held = lax.all_to_all(spread, axis, 0, 0, tiled=True)
        held = held.reshape((-1,) + value.shape)
    return held


def group_gather(value, axis, members):
    count = lax.axis_size(axis)
    own = lax.axis_index(axis)
    held = value[None]
    step = 1
    while step < members:
        pairs = [(source, source ^ step) for source in range(count)]
        other = lax.ppermute(held, axis, pairs)
        low = (own & step) == 0
        held = jnp.where(
            low, jnp.concatenate([held, other], 0), jnp.concatenate([other, held], 0)
        )
        step *= 2
    return held


def local(
    incoming,
    norm_gain,
    query_weight,
    query_scale,
    query_keep,
    kv_weight,
    kv_scale,
    kv_keep,
    out_weight,
    out_scale,
    out_keep,
    documents,
):
    tp = lax.axis_size(TP_AXES)
    own_index = lax.axis_index(TP_AXES)
    planes = lax.axis_size(CROSS)
    plane = lax.axis_size(PLANE)
    local_rows = incoming[0]
    tok_count, own_width = local_rows.shape
    group_size = HEADS // KV_HEADS
    q_width = HEADS * HD // tp
    heads_here = q_width // HD
    members = group_size // heads_here
    chunk = HD // members
    halves = plane // members

    q_eff = dequant(query_weight[0], query_scale[0], query_keep[0])
    q_send = q_eff.reshape(own_width, planes, plane, q_width).transpose(2, 0, 1, 3)
    q_send = q_send.reshape(plane, own_width, planes * q_width)
    kv_eff = dequant(kv_weight[0], kv_scale[0], kv_keep[0])
    kv_send = kv_eff.reshape(own_width, 2, planes, halves, members, chunk)
    kv_send = kv_send.transpose(3, 4, 0, 2, 1, 5).reshape(plane, own_width, planes * 2 * chunk)
    o_eff = dequant(out_weight[0], out_scale[0], out_keep[0])
    o_send = o_eff.reshape(q_width, planes, plane, own_width).transpose(2, 0, 1, 3)
    o_send = o_send.reshape(plane, q_width, planes * own_width)
    both = jnp.concatenate([q_send, kv_send, o_send], axis=2)
    both = lax.all_to_all(both, PLANE, 0, 0, tiled=True).reshape(plane * own_width, -1)
    q_rows = both[:, : planes * q_width]
    kv_rows = both[:, planes * q_width : planes * (q_width + 2 * chunk)]
    o_rows = both[:, planes * (q_width + 2 * chunk) :]

    extended = jnp.concatenate([local_rows, norm_gain[0][None]], axis=0)
    gathered = gather_all(extended, PLANE)
    activ_pl = gathered[:, :tok_count, :].astype(jnp.float32)
    gain_pl = gathered[:, tok_count, :].astype(jnp.float32)
    partial_sq = jnp.sum(activ_pl * activ_pl, axis=(0, 2))
    squares = jnp.sum(gather_all(partial_sq, (CROSS,)), axis=0)
    scale_rows = lax.rsqrt(squares / D + epsilon)
    normed_pl = (activ_pl * scale_rows[None, :, None] * gain_pl[:, None, :]).astype(jnp.bfloat16)
    normed_pl = normed_pl.transpose(1, 0, 2).reshape(tok_count, plane * own_width)

    q_part = jnp.dot(normed_pl, q_rows, preferred_element_type=jnp.float32)
    kv_part = jnp.dot(normed_pl, kv_rows, preferred_element_type=jnp.float32)
    packed = jnp.concatenate(
        [q_part.reshape(tok_count, planes, q_width), kv_part.reshape(tok_count, planes, 2 * chunk)],
        axis=2,
    ).transpose(1, 0, 2)
    summed = jnp.sum(lax.all_to_all(packed, CROSS, 0, 0, tiled=True), axis=0)

    queries = rotate(summed[:, :q_width], own_index * q_width).astype(jnp.bfloat16)
    member = own_index % members
    key_part = rotate(summed[:, q_width : q_width + chunk], member * chunk)
    kv_part = jnp.concatenate([key_part, summed[:, q_width + chunk :]], axis=1).astype(jnp.bfloat16)
    kv_group = group_gather(kv_part, TP_AXES, members)
    key_rows = kv_group[:, :, :chunk].transpose(1, 0, 2).reshape(tok_count, HD)
    value_rows = kv_group[:, :, chunk:].transpose(1, 0, 2).reshape(tok_count, HD)

    token_ids = jnp.arange(tok_count, dtype=jnp.int32)
    allowed = (documents[:, None] == documents[None, :]) & (
        token_ids[:, None] >= token_ids[None, :]
    )
    query_three = queries.reshape(tok_count, heads_here, HD)
    scores = jnp.einsum(
        "thd,sd->hts", query_three, key_rows, preferred_element_type=jnp.float32
    ) / jnp.sqrt(jnp.float32(HD))
    exp_scores = jnp.where(allowed[None], jnp.exp(scores), jnp.float32(0.0))
    probs = (exp_scores / jnp.sum(exp_scores, axis=-1, keepdims=True)).astype(jnp.bfloat16)
    head_out = jnp.einsum("hts,sd->thd", probs, value_rows, preferred_element_type=jnp.float32)
    head_out = head_out.astype(jnp.bfloat16).reshape(tok_count, q_width)

    heads_pl = gather_all(head_out, PLANE).transpose(1, 0, 2).reshape(tok_count, plane * q_width)
    out_part = jnp.dot(heads_pl, o_rows, preferred_element_type=jnp.float32)
    out_part = out_part.reshape(tok_count, planes, own_width).transpose(1, 0, 2)
    mixed_sum = jnp.sum(lax.all_to_all(out_part, CROSS, 0, 0, tiled=True), axis=0)
    layer_out = (local_rows.astype(jnp.float32) + mixed_sum).astype(jnp.bfloat16)
    received = passed_along(layer_out, "section", 1)
    return received[None]


TP_AXES = ("tp_x", "tp_z", "tp_y")
CROSS = "tp_x"
PLANE = ("tp_z", "tp_y")


def solution(mesh):
    devices = mesh.devices.reshape(mesh.shape["section"], 4, 4, -1)
    mesh = Mesh(devices, ("section",) + TP_AXES)
    tp = TP_AXES
    placed = (
        P("section", None, tp),
        P("section", tp),
        P("section", tp, None),
        P("section", tp, None),
        P("section", tp, None),
        P("section", tp, None),
        P("section", tp, None),
        P("section", tp, None),
        P("section", tp, None),
        P("section", tp, None),
        P("section", tp, None),
        P(),
    )
    return jax.shard_map(
        local, mesh=mesh, in_specs=placed, out_specs=P("section", None, tp), check_vma=False
    )
```
